32 devices in a mesh: sub: 8 (over z, x), grp: 4 (over y, core).
Axes of the slice: x: 2, y: 2, z: 4, core: 2. Of those that a mesh axis runs over, the one named last changes fastest.
Arguments:
- resid: float32 [32768, 256], P(('sub', 'grp')), may hold values from -6 to 6
- schur_inv: bfloat16 [65536, 2048], P(('sub', 'grp')), may hold values from -0.125 to 0.125
- basis: bfloat16 [512, 2048], P(('sub', 'grp')), may hold values from -1.5 to 1.5
- scaling: float32 [65536], P(('sub', 'grp')), may hold values from 0.25 to 1
- coarse_inv: bfloat16 [512, 512], P(('sub', 'grp')), may hold values from -0.5 to 0.5
- source_row: int32 [65536], P(('sub', 'grp')), may hold values from 0 to 3071, as said below
- primal_idx: int32 [512], P(('sub', 'grp')), may hold values from 0 to 2047, as said below
Outputs:
- first_apply: float32 [32768, 256], P(('sub', 'grp'))
- second_apply: float32 [32768, 256], P(('sub', 'grp'))
The draws below stay inside these ranges and needn't reach their ends.
Inputs may be any that keep to these rules, and one draw needn't show every extreme that they name: `source_row`: within one subdomain the entries are distinct; the first subdomain of each chain has none below 1024, the last none at or above 2048. `primal_idx`: within one subdomain the entries are distinct.
All inputs are finite; a program needn't handle non-finite values.
Results may differ from the reference program's by a relative error of at most 0.0076.
Values may be sent and summed in bfloat16 or wider, within the bound.
No kernel may reach another device: no remote copies, remote signals or barrier semaphores. Data moves between devices by JAX's collectives and lax.ppermute only.
A program may use at most 64 MiB of HBM per device.

```python
import math
import jax
import jax.numpy as jnp
from jax import lax

LOC = 2048
NP = 16
K = 256
OWN = 1024
CHAIN = 8
GROUPS = 4
SUBDOMAINS = 32
NG = 32768
NC = 512


def draw_source_row(key, part):
    key_perm, key_left, key_right = jax.random.split(jax.random.fold_in(key, 11), 3)
    device_ids = jnp.arange(SUBDOMAINS, dtype=jnp.int32)
    position = device_ids // (SUBDOMAINS // CHAIN)
    orders = jax.vmap(lambda sub_key: jax.random.permutation(sub_key, 3 * OWN).astype(jnp.int32))(jax.random.split(key_perm, SUBDOMAINS))
    region = (jnp.arange(3 * OWN, dtype=jnp.int32) // OWN)[None, :]
    bias_left = jax.random.randint(key_left, (SUBDOMAINS, 1), -(OWN // 2), OWN // 2 + 1, dtype=jnp.int32)
    bias_right = jax.random.randint(key_right, (SUBDOMAINS, 1), -(OWN // 2), OWN // 2 + 1, dtype=jnp.int32)
    bias = jnp.where(region == 0, bias_left, jnp.where(region == 2, bias_right, 0))
    scores = (orders + bias + OWN) * 3 + region
    allowed = ((region != 0) | (position[:, None] > 0)) & ((region != 2) | (position[:, None] < CHAIN - 1))
    scores = jnp.where(allowed, scores, -1)
    chosen = lax.top_k(scores, LOC)[1]
    return chosen.reshape(-1).astype(jnp.int32)


def draw_primal_idx(key, part):
    keys = jax.random.split(jax.random.fold_in(key, 23), SUBDOMAINS)
    picks = jax.vmap(lambda sub_key: jax.random.permutation(sub_key, LOC)[:NP].astype(jnp.int32))(keys)
    return picks.reshape(-1).astype(jnp.int32)


def with_spikes(entries, own_key, source, target, shards_of, factor):
    owner, partner = [(jnp.arange(entries.shape[axis_at]) // (entries.shape[axis_at] // shards_of)).reshape([-1 if axis == axis_at else 1 for axis in range(entries.ndim)]) for axis_at in (source, target)]
    chosen = jax.random.permutation(own_key, shards_of)[partner]
    strong = (owner == chosen) | (owner == (partner + shards_of // 2) % shards_of)
    return jnp.where(strong, factor * entries, entries)


def levels(key, shape, pieces, smallest, high):
    level, own = 1.0, jax.random.fold_in(key, 6)
    for dim, shards_of in pieces:
        steps = jnp.exp(jax.random.uniform(jax.random.fold_in(own, dim), (shards_of,), jnp.float32, smallest / len(pieces), high / len(pieces)))
        level = level * jnp.repeat(steps, shape[dim] // shards_of).reshape([-1 if axis == dim else 1 for axis in range(len(shape))])
    return level


def centred(rng, extent, width, limit, pieces=(), kind=jnp.bfloat16):
    entries = jax.random.normal(rng, extent, jnp.float32) * width
    if len(pieces) > 0:
        entries = levels(rng, extent, pieces, -0.22, 0.18) * entries
    return jnp.clip(entries, min=-limit, max=limit).astype(kind)


def gaussian_with(key, shape, deviation, most, cuts, heavy, kind=jnp.bfloat16):
    entries = deviation * jax.random.normal(key, shape, jnp.float32)
    if cuts:
        entries = entries * levels(key, shape, cuts, -0.22, 0.18)
    return jnp.clip(with_spikes(entries, jax.random.fold_in(key, 3), *heavy), -most, most).astype(kind)


def setup_inputs(seed: int = 0) -> dict:
    key_of = jax.random.split(jax.random.key(seed), 8)
    return {
        "resid": centred(key_of[0], (NG, K), 1.0, 6.0, ((0, 32),), jnp.float32),
        "schur_inv": centred(key_of[1], (SUBDOMAINS * LOC, LOC), LOC ** -0.5, 0.125, ((0, 32),)),
        "basis": centred(key_of[2], (SUBDOMAINS * NP, LOC), NP ** -0.5, 1.5, ((0, 32),)),
        "scaling": jnp.clip(jnp.exp(math.log(1.0) - 1.3862944 * jax.random.uniform(key_of[3], (SUBDOMAINS * LOC,), jnp.float32) ** levels(key_of[3], (SUBDOMAINS * LOC,), ((0, 32),), -0.2, 0.2)), 0.25, 1.0),
        "coarse_inv": gaussian_with(key_of[4], (NC, NC), NC ** -0.5, 0.5, ((0, 32),), (1, 0, 32, 2.75)),
        "source_row": draw_source_row(jax.random.fold_in(key_of[7], 71), 0),
        "primal_idx": draw_primal_idx(jax.random.fold_in(key_of[7], 71), 0),
    }


def reference(resid, schur_inv, basis, scaling, coarse_inv, source_row, primal_idx):
    sources = source_row.reshape(SUBDOMAINS, LOC)
    device_ids = jnp.arange(SUBDOMAINS, dtype=jnp.int32)[:, None]
    row_map = ((device_ids + (sources // OWN - 1) * GROUPS) * OWN + sources % OWN).astype(jnp.int32)
    primal_rows = primal_idx.reshape(SUBDOMAINS, NP).astype(jnp.int32)
    row_scale = scaling.reshape(SUBDOMAINS, LOC, 1)
    matrices = schur_inv.reshape(SUBDOMAINS, LOC, LOC)
    bases = basis.reshape(SUBDOMAINS, NP, LOC)

    def solve_one(members):
        matrix, vector, basis_rows, correction = members
        return jnp.dot(matrix, vector, preferred_element_type=jnp.float32) + jnp.dot(basis_rows.T, correction, preferred_element_type=jnp.float32)

    def precondition(vector_in):
        rounded = vector_in.astype(jnp.bfloat16)
        gathered = rounded[row_map]
        scaled = (row_scale * gathered.astype(jnp.float32)).astype(jnp.bfloat16)
        primal = jax.vmap(lambda rows_all, picks: rows_all[picks])(scaled, primal_rows)
        coarse = jnp.dot(coarse_inv, primal.reshape(NC, K), preferred_element_type=jnp.float32).astype(jnp.bfloat16)
        coarse = coarse.reshape(SUBDOMAINS, NP, K)
        solved = lax.map(solve_one, (matrices, scaled, bases, coarse))
        weighted = (row_scale * solved).astype(jnp.bfloat16)
        summed = jnp.zeros((NG, K), jnp.float32)
        return summed.at[row_map.reshape(-1)].add(weighted.reshape(-1, K).astype(jnp.float32))

    first_apply = precondition(resid)
    second_apply = precondition(first_apply)
    return (first_apply, second_apply)
```

```python
import jax
import jax.numpy as jnp
from jax import lax
from jax.sharding import PartitionSpec as P


def with_halo(cells, sides, width):
    for axis, dim in sides:
        count = lax.axis_size(axis)
        ends = count - 1
        head = lax.slice_in_dim(cells, 0, width, axis=dim)
        tail = lax.slice_in_dim(cells, cells.shape[dim] - width, cells.shape[dim], axis=dim)
        cells = jnp.concatenate(
            [
                lax.ppermute(tail, axis, [(i, (i + 1) % count) for i in range(ends)]),
                cells,
                lax.ppermute(head, axis, [((i + 1) % count, i) for i in range(ends)]),
            ],
            axis=dim,
        )
    return cells


def shifted(shard, axis, by):
    devices = lax.axis_size(axis)
    pairs = [(i, i + by) for i in range(devices) if 0 <= i + by < devices]
    return lax.ppermute(shard, axis, pairs)


def shards(resid, schur_inv, basis, scaling, coarse_inv, source_row, primal_idx):
    own_count = resid.shape[0]
    scale_column = scaling[:, None]

    def add_all(portion):
        return jnp.dot(coarse_inv, portion, preferred_element_type=jnp.float32)

    def precondition(vector_in):
        rounded = vector_in.astype(jnp.bfloat16)
        padded = with_halo(rounded, (("sub", 0),), own_count)
        gathered = padded[source_row]
        scaled = (scale_column * gathered.astype(jnp.float32)).astype(jnp.bfloat16)
        primal = scaled[primal_idx]
        idx = lax.axis_index("sub") * lax.axis_size("grp") + lax.axis_index("grp")
        total = lax.axis_size("sub") * lax.axis_size("grp") * primal.shape[0]
        buf = lax.dynamic_update_slice(jnp.zeros((total, primal.shape[1]), primal.dtype), primal, (idx * primal.shape[0], 0))
        coarse = add_all(lax.psum(buf, ("sub", "grp")))
        coarse_rounded = coarse.astype(jnp.bfloat16)
        solved = jnp.dot(schur_inv, scaled, preferred_element_type=jnp.float32)
        solved = solved + lax.dot_general(
            basis, coarse_rounded, (((0,), (0,)), ((), ())), preferred_element_type=jnp.float32
        )
        weighted = (scale_column * solved).astype(jnp.bfloat16)
        spread = (
            jnp.zeros((3 * own_count, weighted.shape[1]), jnp.bfloat16).at[source_row].set(weighted)
        )
        from_next = shifted(spread[:own_count], "sub", -1)
        from_previous = shifted(spread[2 * own_count :], "sub", 1)
        return (
            spread[own_count : 2 * own_count].astype(jnp.float32)
            + from_next.astype(jnp.float32)
            + from_previous.astype(jnp.float32)
        )

    first_apply = precondition(resid)
    second_apply = precondition(first_apply)
    return (first_apply, second_apply)


def solution(mesh):
    return jax.shard_map(
        shards,
        mesh=mesh,
        in_specs=(
            P(("sub", "grp"), None),
            P(("sub", "grp"), None),
            P(("sub", "grp"), None),
            P(("sub", "grp")),
            P(("sub", "grp"), None),
            P(("sub", "grp")),
            P(("sub", "grp")),
        ),
        out_specs=(P(("sub", "grp"), None), P(("sub", "grp"), None)),
        check_vma=False,
    )
```

```python
import jax
import jax.numpy as jnp
from jax import lax
from jax.sharding import PartitionSpec as P

AXES = ("sub", "grp")


def with_halo(cells, sides, width):
    for axis, dim in sides:
        count = lax.axis_size(axis)
        ends = count - 1
        head = lax.slice_in_dim(cells, 0, width, axis=dim)
        tail = lax.slice_in_dim(cells, cells.shape[dim] - width, cells.shape[dim], axis=dim)
        cells = jnp.concatenate(
            [
                lax.ppermute(tail, axis, [(i, (i + 1) % count) for i in range(ends)]),
                cells,
                lax.ppermute(head, axis, [((i + 1) % count, i) for i in range(ends)]),
            ],
            axis=dim,
        )
    return cells


def shifted(shard, axis, by):
    devices = lax.axis_size(axis)
    pairs = [(i, i + by) for i in range(devices) if 0 <= i + by < devices]
    return lax.ppermute(shard, axis, pairs)


def gather_all(block):
    count = lax.axis_size("sub") * lax.axis_size("grp")
    me = lax.axis_index("sub") * lax.axis_size("grp") + lax.axis_index("grp")
    rows = block.shape[0]
    held = lax.dynamic_update_slice_in_dim(
        jnp.zeros((count * rows, block.shape[1]), block.dtype), block, me * rows, 0
    )
    span = 1
    while span < count:
        start = (me // span) * span
        piece = lax.dynamic_slice_in_dim(held, start * rows, span * rows, 0)
        got = lax.ppermute(piece, AXES, [(i, i ^ span) for i in range(count)])
        held = lax.dynamic_update_slice_in_dim(held, got, (start ^ span) * rows, 0)
        span *= 2
    return held


CHUNKS = 4


def shards(resid, schur_inv, basis, scaling, coarse_inv, source_row, primal_idx):
    own_count = resid.shape[0]
    scale_column = scaling[:, None]

    def precondition(vector_in):
        rounded = vector_in.astype(jnp.bfloat16)
        padded = with_halo(rounded, (("sub", 0),), own_count)
        gathered = padded[source_row]
        scaled = (scale_column * gathered.astype(jnp.float32)).astype(jnp.bfloat16)
        primal = scaled[primal_idx]
        coarse = jnp.dot(coarse_inv, gather_all(primal), preferred_element_type=jnp.float32)
        coarse_rounded = coarse.astype(jnp.bfloat16)
        solved = jnp.dot(schur_inv, scaled, preferred_element_type=jnp.float32)
        solved = solved + lax.dot_general(
            basis, coarse_rounded, (((0,), (0,)), ((), ())), preferred_element_type=jnp.float32
        )
        weighted = (scale_column * solved).astype(jnp.bfloat16)
        spread = (
            jnp.zeros((3 * own_count, weighted.shape[1]), jnp.bfloat16).at[source_row].set(weighted)
        )
        from_next = shifted(spread[:own_count], "sub", -1)
        from_previous = shifted(spread[2 * own_count :], "sub", 1)
        return (
            spread[own_count : 2 * own_count].astype(jnp.float32)
            + from_next.astype(jnp.float32)
            + from_previous.astype(jnp.float32)
        )

    width = resid.shape[1] // CHUNKS
    firsts, seconds = [], []
    for c in range(CHUNKS):
        first = precondition(resid[:, c * width : (c + 1) * width])
        firsts.append(first)
        seconds.append(precondition(first))
    return (jnp.concatenate(firsts, axis=1), jnp.concatenate(seconds, axis=1))


def solution(mesh):
    return jax.shard_map(
        shards,
        mesh=mesh,
        in_specs=(
            P(AXES, None),
            P(AXES, None),
            P(AXES, None),
            P(AXES),
            P(AXES, None),
            P(AXES),
            P(AXES),
        ),
        out_specs=(P(AXES, None), P(AXES, None)),
        check_vma=False,
    )
```

```python
import jax
import jax.numpy as jnp
from jax import lax
from jax.sharding import PartitionSpec as P

AXES = ("sub", "grp")


def with_halo(cells, sides, width):
    for axis, dim in sides:
        count = lax.axis_size(axis)
        ends = count - 1
        head = lax.slice_in_dim(cells, 0, width, axis=dim)
        tail = lax.slice_in_dim(cells, cells.shape[dim] - width, cells.shape[dim], axis=dim)
        cells = jnp.concatenate(
            [
                lax.ppermute(tail, axis, [(i, (i + 1) % count) for i in range(ends)]),
                cells,
                lax.ppermute(head, axis, [((i + 1) % count, i) for i in range(ends)]),
            ],
            axis=dim,
        )
    return cells


def shifted(shard, axis, by):
    devices = lax.axis_size(axis)
    pairs = [(i, i + by) for i in range(devices) if 0 <= i + by < devices]
    return lax.ppermute(shard, axis, pairs)


def gather_all(block):
    count = lax.axis_size("sub") * lax.axis_size("grp")
    me = lax.axis_index("sub") * lax.axis_size("grp") + lax.axis_index("grp")
    rows = block.shape[0]
    held = lax.dynamic_update_slice_in_dim(
        jnp.zeros((count * rows, block.shape[1]), block.dtype), block, me * rows, 0
    )
    span = 1
    while span < count:
        start = (me // span) * span
        piece = lax.dynamic_slice_in_dim(held, start * rows, span * rows, 0)
        got = lax.ppermute(piece, AXES, [(i, i ^ span) for i in range(count)])
        held = lax.dynamic_update_slice_in_dim(held, got, (start ^ span) * rows, 0)
        span *= 2
    return held


def shards(resid, schur_inv, basis, scaling, coarse_inv, source_row, primal_idx):
    own_count = resid.shape[0]
    scale_column = scaling[:, None]

    primal_source = source_row[primal_idx]
    region = primal_source // own_count
    offset = primal_source % own_count
    primal_scale = scaling[primal_idx]
    asks_previous = jnp.stack([jnp.where(region == 0, offset, 0).astype(jnp.float32), primal_scale])
    asks_next = jnp.stack([jnp.where(region == 2, offset, 0).astype(jnp.float32), primal_scale])
    asked_by_next = shifted(asks_previous, "sub", -1)
    asked_by_previous = shifted(asks_next, "sub", 1)
    own_offset = jnp.where(region == 1, offset, 0)

    def primal_rows(rounded, rows, scale):
        return (scale[:, None] * rounded[rows].astype(jnp.float32)).astype(jnp.bfloat16)

    def precondition(vector_in):
        rounded = vector_in.astype(jnp.bfloat16)
        for_next = primal_rows(rounded, asked_by_next[0].astype(jnp.int32), asked_by_next[1])
        for_previous = primal_rows(rounded, asked_by_previous[0].astype(jnp.int32), asked_by_previous[1])
        from_previous_owner = shifted(for_next, "sub", 1)
        from_next_owner = shifted(for_previous, "sub", -1)
        mine = primal_rows(rounded, own_offset, primal_scale)
        primal = jnp.where(
            (region == 1)[:, None], mine,
            jnp.where((region == 0)[:, None], from_previous_owner, from_next_owner),
        )
        primal_all = gather_all(primal)

        padded = with_halo(rounded, (("sub", 0),), own_count)
        gathered = padded[source_row]
        scaled = (scale_column * gathered.astype(jnp.float32)).astype(jnp.bfloat16)
        coarse = jnp.dot(coarse_inv, primal_all, preferred_element_type=jnp.float32)
        coarse_rounded = coarse.astype(jnp.bfloat16)
        solved = jnp.dot(schur_inv, scaled, preferred_element_type=jnp.float32)
        solved = solved + lax.dot_general(
            basis, coarse_rounded, (((0,), (0,)), ((), ())), preferred_element_type=jnp.float32
        )
        weighted = (scale_column * solved).astype(jnp.bfloat16)
        spread = (
            jnp.zeros((3 * own_count, weighted.shape[1]), jnp.bfloat16).at[source_row].set(weighted)
        )
        from_next = shifted(spread[:own_count], "sub", -1)
        from_previous = shifted(spread[2 * own_count :], "sub", 1)
        return (
            spread[own_count : 2 * own_count].astype(jnp.float32)
            + from_next.astype(jnp.float32)
            + from_previous.astype(jnp.float32)
        )

    first_apply = precondition(resid)
    second_apply = precondition(first_apply)
    return (first_apply, second_apply)


def solution(mesh):
    return jax.shard_map(
        shards,
        mesh=mesh,
        in_specs=(
            P(AXES, None),
            P(AXES, None),
            P(AXES, None),
            P(AXES),
            P(AXES, None),
            P(AXES),
            P(AXES),
        ),
        out_specs=(P(AXES, None), P(AXES, None)),
        check_vma=False,
    )
```

```python
import jax
import jax.numpy as jnp
from jax import lax
from jax.sharding import PartitionSpec as P

AXES = ("sub", "grp")


def with_halo(cells, sides, width):
    for axis, dim in sides:
        count = lax.axis_size(axis)
        ends = count - 1
        head = lax.slice_in_dim(cells, 0, width, axis=dim)
        tail = lax.slice_in_dim(cells, cells.shape[dim] - width, cells.shape[dim], axis=dim)
        cells = jnp.concatenate(
            [
                lax.ppermute(tail, axis, [(i, (i + 1) % count) for i in range(ends)]),
                cells,
                lax.ppermute(head, axis, [((i + 1) % count, i) for i in range(ends)]),
            ],
            axis=dim,
        )
    return cells


def shifted(shard, axis, by):
    devices = lax.axis_size(axis)
    pairs = [(i, i + by) for i in range(devices) if 0 <= i + by < devices]
    return lax.ppermute(shard, axis, pairs)


def gather_all(block):
    count = lax.axis_size("sub") * lax.axis_size("grp")
    me = lax.axis_index("sub") * lax.axis_size("grp") + lax.axis_index("grp")
    rows = block.shape[0]
    held = lax.dynamic_update_slice_in_dim(
        jnp.zeros((count * rows, block.shape[1]), block.dtype), block, me * rows, 0
    )
    span = 1
    while span < count:
        start = (me // span) * span
        piece = lax.dynamic_slice_in_dim(held, start * rows, span * rows, 0)
        got = lax.ppermute(piece, AXES, [(i, i ^ span) for i in range(count)])
        held = lax.dynamic_update_slice_in_dim(held, got, (start ^ span) * rows, 0)
        span *= 2
    return held


def shards(resid, schur_inv, basis, scaling, coarse_inv, source_row, primal_idx):
    own_count = resid.shape[0]
    scale_column = scaling[:, None]
    primal_source = source_row[primal_idx]
    primal_scale = scaling[primal_idx][:, None]

    def precondition(vector_in):
        rounded = vector_in.astype(jnp.bfloat16)
        padded = with_halo(rounded, (("sub", 0),), own_count)
        primal = (primal_scale * padded[primal_source].astype(jnp.float32)).astype(jnp.bfloat16)
        primal_all = gather_all(primal)
        gathered = padded[source_row]
        scaled = (scale_column * gathered.astype(jnp.float32)).astype(jnp.bfloat16)
        solved = jnp.dot(schur_inv, scaled, preferred_element_type=jnp.float32)
        solved = lax.optimization_barrier(solved)
        coarse = jnp.dot(coarse_inv, primal_all, preferred_element_type=jnp.float32)
        coarse_rounded = coarse.astype(jnp.bfloat16)
        solved = solved + lax.dot_general(
            basis, coarse_rounded, (((0,), (0,)), ((), ())), preferred_element_type=jnp.float32
        )
        weighted = (scale_column * solved).astype(jnp.bfloat16)
        spread = (
            jnp.zeros((3 * own_count, weighted.shape[1]), jnp.bfloat16).at[source_row].set(weighted)
        )
        from_next = shifted(spread[:own_count], "sub", -1)
        from_previous = shifted(spread[2 * own_count :], "sub", 1)
        return (
            spread[own_count : 2 * own_count].astype(jnp.float32)
            + from_next.astype(jnp.float32)
            + from_previous.astype(jnp.float32)
        )

    first_apply = precondition(resid)
    second_apply = precondition(first_apply)
    return (first_apply, second_apply)


def solution(mesh):
    return jax.shard_map(
        shards,
        mesh=mesh,
        in_specs=(
            P(AXES, None),
            P(AXES, None),
            P(AXES, None),
            P(AXES),
            P(AXES, None),
            P(AXES),
            P(AXES),
        ),
        out_specs=(P(AXES, None), P(AXES, None)),
        check_vma=False,
    )
```

```python
import jax
import jax.numpy as jnp
from jax import lax
from jax.sharding import PartitionSpec as P

AXES = ("sub", "grp")


def with_halo(cells, sides, width):
    for axis, dim in sides:
        count = lax.axis_size(axis)
        ends = count - 1
        head = lax.slice_in_dim(cells, 0, width, axis=dim)
        tail = lax.slice_in_dim(cells, cells.shape[dim] - width, cells.shape[dim], axis=dim)
        cells = jnp.concatenate(
            [
                lax.ppermute(tail, axis, [(i, (i + 1) % count) for i in range(ends)]),
                cells,
                lax.ppermute(head, axis, [((i + 1) % count, i) for i in range(ends)]),
            ],
            axis=dim,
        )
    return cells


def shifted(shard, axis, by):
    devices = lax.axis_size(axis)
    pairs = [(i, i + by) for i in range(devices) if 0 <= i + by < devices]
    return lax.ppermute(shard, axis, pairs)


def gather_all(block):
    count = lax.axis_size("sub") * lax.axis_size("grp")
    me = lax.axis_index("sub") * lax.axis_size("grp") + lax.axis_index("grp")
    rows = block.shape[0]
    held = lax.dynamic_update_slice_in_dim(
        jnp.zeros((count * rows, block.shape[1]), block.dtype), block, me * rows, 0
    )
    span = 1
    while span < count:
        start = (me // span) * span
        piece = lax.dynamic_slice_in_dim(held, start * rows, span * rows, 0)
        got = lax.ppermute(piece, AXES, [(i, i ^ span) for i in range(count)])
        held = lax.dynamic_update_slice_in_dim(held, got, (start ^ span) * rows, 0)
        span *= 2
    return held


def shards(resid, schur_inv, basis, scaling, coarse_inv, source_row, primal_idx):
    own_count = resid.shape[0]
    scale_column = scaling[:, None]
    primal_source = source_row[primal_idx]
    primal_scale = scaling[primal_idx][:, None]

    picks = [
        (source_row[:, None] == (region * own_count + jnp.arange(own_count))[None, :]).astype(jnp.bfloat16)
        for region in range(3)
    ]
    places = [
        ((region * own_count + jnp.arange(own_count))[:, None] == source_row[None, :]).astype(jnp.bfloat16)
        for region in range(3)
    ]

    def select(matrix, rows):
        return jnp.dot(matrix, rows, preferred_element_type=jnp.float32)

    def precondition(vector_in):
        rounded = vector_in.astype(jnp.bfloat16)
        padded = with_halo(rounded, (("sub", 0),), own_count)
        before = padded[:own_count]
        after = padded[2 * own_count :]
        primal = (primal_scale * padded[primal_source].astype(jnp.float32)).astype(jnp.bfloat16)
        primal_all = gather_all(primal)
        gathered = select(picks[1], rounded) + select(picks[0], before) + select(picks[2], after)
        scaled = (scale_column * gathered).astype(jnp.bfloat16)
        solved = jnp.dot(schur_inv, scaled, preferred_element_type=jnp.float32)
        solved = lax.optimization_barrier(solved)
        coarse = jnp.dot(coarse_inv, primal_all, preferred_element_type=jnp.float32)
        coarse_rounded = coarse.astype(jnp.bfloat16)
        solved = solved + lax.dot_general(
            basis, coarse_rounded, (((0,), (0,)), ((), ())), preferred_element_type=jnp.float32
        )
        weighted = (scale_column * solved).astype(jnp.bfloat16)
        to_previous = select(places[0], weighted).astype(jnp.bfloat16)
        to_next = select(places[2], weighted).astype(jnp.bfloat16)
        from_next = shifted(to_previous, "sub", -1)
        from_previous = shifted(to_next, "sub", 1)
        kept = select(places[1], weighted).astype(jnp.bfloat16)
        return (
            kept.astype(jnp.float32)
            + from_next.astype(jnp.float32)
            + from_previous.astype(jnp.float32)
        )

    first_apply = precondition(resid)
    second_apply = precondition(first_apply)
    return (first_apply, second_apply)


def solution(mesh):
    return jax.shard_map(
        shards,
        mesh=mesh,
        in_specs=(
            P(AXES, None),
            P(AXES, None),
            P(AXES, None),
            P(AXES),
            P(AXES, None),
            P(AXES),
            P(AXES),
        ),
        out_specs=(P(AXES, None), P(AXES, None)),
        check_vma=False,
    )
```

```python
import jax
import jax.numpy as jnp
from jax import lax
from jax.sharding import PartitionSpec as P

AXES = ("sub", "grp")


def with_halo(cells, sides, width):
    for axis, dim in sides:
        count = lax.axis_size(axis)
        ends = count - 1
        head = lax.slice_in_dim(cells, 0, width, axis=dim)
        tail = lax.slice_in_dim(cells, cells.shape[dim] - width, cells.shape[dim], axis=dim)
        cells = jnp.concatenate(
            [
                lax.ppermute(tail, axis, [(i, (i + 1) % count) for i in range(ends)]),
                cells,
                lax.ppermute(head, axis, [((i + 1) % count, i) for i in range(ends)]),
            ],
            axis=dim,
        )
    return cells


def shifted(shard, axis, by):
    devices = lax.axis_size(axis)
    pairs = [(i, i + by) for i in range(devices) if 0 <= i + by < devices]
    return lax.ppermute(shard, axis, pairs)


def gather_all(block):
    count = lax.axis_size("sub") * lax.axis_size("grp")
    me = lax.axis_index("sub") * lax.axis_size("grp") + lax.axis_index("grp")
    rows = block.shape[0]
    held = lax.dynamic_update_slice_in_dim(
        jnp.zeros((count * rows, block.shape[1]), block.dtype), block, me * rows, 0
    )
    span = 1
    while span < count:
        start = (me // span) * span
        piece = lax.dynamic_slice_in_dim(held, start * rows, span * rows, 0)
        got = lax.ppermute(piece, AXES, [(i, i ^ span) for i in range(count)])
        held = lax.dynamic_update_slice_in_dim(held, got, (start ^ span) * rows, 0)
        span *= 2
    return held


def shards(resid, schur_inv, basis, scaling, coarse_inv, source_row, primal_idx):
    own_count = resid.shape[0]
    scale_column = scaling[:, None]
    primal_source = source_row[primal_idx]
    primal_scale = scaling[primal_idx][:, None]

    picks = [
        (source_row[:, None] == (region * own_count + jnp.arange(own_count))[None, :]).astype(jnp.bfloat16)
        for region in range(3)
    ]
    places = [
        ((region * own_count + jnp.arange(own_count))[:, None] == source_row[None, :]).astype(jnp.bfloat16)
        for region in range(3)
    ]

    def select(matrix, rows):
        return jnp.dot(matrix, rows, preferred_element_type=jnp.float32)

    def precondition(vector_in):
        rounded = vector_in.astype(jnp.bfloat16)
        padded = with_halo(rounded, (("sub", 0),), own_count)
        before = padded[:own_count]
        after = padded[2 * own_count :]
        primal = (primal_scale * padded[primal_source].astype(jnp.float32)).astype(jnp.bfloat16)
        count = lax.axis_size("sub") * lax.axis_size("grp")
        primal_all = lax.all_to_all(
            jnp.broadcast_to(primal[None], (count,) + primal.shape), AXES, 0, 0, tiled=False
        ).reshape(-1, primal.shape[1])
        gathered = select(picks[1], rounded) + select(picks[0], before) + select(picks[2], after)
        scaled = (scale_column * gathered).astype(jnp.bfloat16)
        solved = jnp.dot(schur_inv, scaled, preferred_element_type=jnp.float32)
        solved = lax.optimization_barrier(solved)
        coarse = jnp.dot(coarse_inv, primal_all, preferred_element_type=jnp.float32)
        coarse_rounded = coarse.astype(jnp.bfloat16)
        solved = solved + lax.dot_general(
            basis, coarse_rounded, (((0,), (0,)), ((), ())), preferred_element_type=jnp.float32
        )
        weighted = (scale_column * solved).astype(jnp.bfloat16)
        to_previous = select(places[0], weighted).astype(jnp.bfloat16)
        to_next = select(places[2], weighted).astype(jnp.bfloat16)
        from_next = shifted(to_previous, "sub", -1)
        from_previous = shifted(to_next, "sub", 1)
        kept = select(places[1], weighted).astype(jnp.bfloat16)
        return (
            kept.astype(jnp.float32)
            + from_next.astype(jnp.float32)
            + from_previous.astype(jnp.float32)
        )

    first_apply = precondition(resid)
    second_apply = precondition(first_apply)
    return (first_apply, second_apply)


def solution(mesh):
    return jax.shard_map(
        shards,
        mesh=mesh,
        in_specs=(
            P(AXES, None),
            P(AXES, None),
            P(AXES, None),
            P(AXES),
            P(AXES, None),
            P(AXES),
            P(AXES),
        ),
        out_specs=(P(AXES, None), P(AXES, None)),
        check_vma=False,
    )
```

```python
import jax
import jax.numpy as jnp
from jax import lax
from jax.sharding import PartitionSpec as P

AXES = ("sub", "grp")


def with_halo(cells, sides, width):
    for axis, dim in sides:
        count = lax.axis_size(axis)
        ends = count - 1
        head = lax.slice_in_dim(cells, 0, width, axis=dim)
        tail = lax.slice_in_dim(cells, cells.shape[dim] - width, cells.shape[dim], axis=dim)
        cells = jnp.concatenate(
            [
                lax.ppermute(tail, axis, [(i, (i + 1) % count) for i in range(ends)]),
                cells,
                lax.ppermute(head, axis, [((i + 1) % count, i) for i in range(ends)]),
            ],
            axis=dim,
        )
    return cells


def shifted(shard, axis, by):
    devices = lax.axis_size(axis)
    pairs = [(i, i + by) for i in range(devices) if 0 <= i + by < devices]
    return lax.ppermute(shard, axis, pairs)


def gather_all(block):
    count = lax.axis_size("sub") * lax.axis_size("grp")
    me = lax.axis_index("sub") * lax.axis_size("grp") + lax.axis_index("grp")
    rows = block.shape[0]
    held = lax.dynamic_update_slice_in_dim(
        jnp.zeros((count * rows, block.shape[1]), block.dtype), block, me * rows, 0
    )
    span = 1
    while span < count:
        start = (me // span) * span
        piece = lax.dynamic_slice_in_dim(held, start * rows, span * rows, 0)
        got = lax.ppermute(piece, AXES, [(i, i ^ span) for i in range(count)])
        held = lax.dynamic_update_slice_in_dim(held, got, (start ^ span) * rows, 0)
        span *= 2
    return held


CHUNKS = 2


def shards(resid, schur_inv, basis, scaling, coarse_inv, source_row, primal_idx):
    own_count = resid.shape[0]
    scale_column = scaling[:, None]
    primal_source = source_row[primal_idx]
    primal_scale = scaling[primal_idx][:, None]

    picks = [
        (source_row[:, None] == (region * own_count + jnp.arange(own_count))[None, :]).astype(jnp.bfloat16)
        for region in range(3)
    ]
    places = [
        ((region * own_count + jnp.arange(own_count))[:, None] == source_row[None, :]).astype(jnp.bfloat16)
        for region in range(3)
    ]

    def select(matrix, rows):
        return jnp.dot(matrix, rows, preferred_element_type=jnp.float32)

    def precondition(vector_in):
        rounded = vector_in.astype(jnp.bfloat16)
        padded = with_halo(rounded, (("sub", 0),), own_count)
        before = padded[:own_count]
        after = padded[2 * own_count :]
        primal = (primal_scale * padded[primal_source].astype(jnp.float32)).astype(jnp.bfloat16)
        count = lax.axis_size("sub") * lax.axis_size("grp")
        primal_all = lax.all_to_all(
            jnp.broadcast_to(primal[None], (count,) + primal.shape), AXES, 0, 0, tiled=False
        ).reshape(-1, primal.shape[1])
        gathered = select(picks[1], rounded) + select(picks[0], before) + select(picks[2], after)
        scaled = (scale_column * gathered).astype(jnp.bfloat16)
        solved = jnp.dot(schur_inv, scaled, preferred_element_type=jnp.float32)
        solved = lax.optimization_barrier(solved)
        coarse = jnp.dot(coarse_inv, primal_all, preferred_element_type=jnp.float32)
        coarse_rounded = coarse.astype(jnp.bfloat16)
        solved = solved + lax.dot_general(
            basis, coarse_rounded, (((0,), (0,)), ((), ())), preferred_element_type=jnp.float32
        )
        weighted = (scale_column * solved).astype(jnp.bfloat16)
        to_previous = select(places[0], weighted).astype(jnp.bfloat16)
        to_next = select(places[2], weighted).astype(jnp.bfloat16)
        from_next = shifted(to_previous, "sub", -1)
        from_previous = shifted(to_next, "sub", 1)
        kept = select(places[1], weighted).astype(jnp.bfloat16)
        return (
            kept.astype(jnp.float32)
            + from_next.astype(jnp.float32)
            + from_previous.astype(jnp.float32)
        )

    width = resid.shape[1] // CHUNKS
    firsts, seconds = [], []
    for c in range(CHUNKS):
        first = precondition(resid[:, c * width : (c + 1) * width])
        firsts.append(first)
        seconds.append(precondition(first))
    return (jnp.concatenate(firsts, axis=1), jnp.concatenate(seconds, axis=1))


def solution(mesh):
    return jax.shard_map(
        shards,
        mesh=mesh,
        in_specs=(
            P(AXES, None),
            P(AXES, None),
            P(AXES, None),
            P(AXES),
            P(AXES, None),
            P(AXES),
            P(AXES),
        ),
        out_specs=(P(AXES, None), P(AXES, None)),
        check_vma=False,
    )
```

```python
import jax
import jax.numpy as jnp
from jax import lax
from jax.sharding import PartitionSpec as P

AXES = ("sub", "grp")


def with_halo(cells, sides, width):
    for axis, dim in sides:
        count = lax.axis_size(axis)
        ends = count - 1
        head = lax.slice_in_dim(cells, 0, width, axis=dim)
        tail = lax.slice_in_dim(cells, cells.shape[dim] - width, cells.shape[dim], axis=dim)
        cells = jnp.concatenate(
            [
                lax.ppermute(tail, axis, [(i, (i + 1) % count) for i in range(ends)]),
                cells,
                lax.ppermute(head, axis, [((i + 1) % count, i) for i in range(ends)]),
            ],
            axis=dim,
        )
    return cells


def shifted(shard, axis, by):
    devices = lax.axis_size(axis)
    pairs = [(i, i + by) for i in range(devices) if 0 <= i + by < devices]
    return lax.ppermute(shard, axis, pairs)


def gather_all(block):
    count = lax.axis_size("sub") * lax.axis_size("grp")
    me = lax.axis_index("sub") * lax.axis_size("grp") + lax.axis_index("grp")
    rows = block.shape[0]
    held = lax.dynamic_update_slice_in_dim(
        jnp.zeros((count * rows, block.shape[1]), block.dtype), block, me * rows, 0
    )
    span = 1
    while span < count:
        start = (me // span) * span
        piece = lax.dynamic_slice_in_dim(held, start * rows, span * rows, 0)
        got = lax.ppermute(piece, AXES, [(i, i ^ span) for i in range(count)])
        held = lax.dynamic_update_slice_in_dim(held, got, (start ^ span) * rows, 0)
        span *= 2
    return held


def shards(resid, schur_inv, basis, scaling, coarse_inv, source_row, primal_idx):
    own_count = resid.shape[0]
    scale_column = scaling[:, None]
    primal_source = source_row[primal_idx]
    primal_scale = scaling[primal_idx][:, None]

    padded_rows = jnp.arange(3 * own_count)
    pick = (source_row[:, None] == padded_rows[None, :]).astype(jnp.bfloat16)
    place = (padded_rows[:, None] == source_row[None, :]).astype(jnp.bfloat16)
    pick, place = lax.optimization_barrier((pick, place))

    def select(matrix, rows):
        return jnp.dot(matrix, rows, preferred_element_type=jnp.float32)

    def precondition(vector_in):
        rounded = vector_in.astype(jnp.bfloat16)
        padded = with_halo(rounded, (("sub", 0),), own_count)
        primal = (primal_scale * padded[primal_source].astype(jnp.float32)).astype(jnp.bfloat16)
        count = lax.axis_size("sub") * lax.axis_size("grp")
        primal_all = lax.all_to_all(
            jnp.broadcast_to(primal[None], (count,) + primal.shape), AXES, 0, 0, tiled=False
        ).reshape(-1, primal.shape[1])
        gathered = select(pick, padded)
        scaled = (scale_column * gathered).astype(jnp.bfloat16)
        solved = jnp.dot(schur_inv, scaled, preferred_element_type=jnp.float32)
        solved = lax.optimization_barrier(solved)
        coarse = jnp.dot(coarse_inv, primal_all, preferred_element_type=jnp.float32)
        coarse_rounded = coarse.astype(jnp.bfloat16)
        solved = solved + lax.dot_general(
            basis, coarse_rounded, (((0,), (0,)), ((), ())), preferred_element_type=jnp.float32
        )
        weighted = (scale_column * solved).astype(jnp.bfloat16)
        to_previous = select(place[:own_count], weighted).astype(jnp.bfloat16)
        to_next = select(place[2 * own_count :], weighted).astype(jnp.bfloat16)
        from_next = shifted(to_previous, "sub", -1)
        from_previous = shifted(to_next, "sub", 1)
        kept = lax.optimization_barrier(select(place[own_count : 2 * own_count], weighted).astype(jnp.bfloat16))
        return (
            kept.astype(jnp.float32)
            + from_next.astype(jnp.float32)
            + from_previous.astype(jnp.float32)
        )

    first_apply = precondition(resid)
    second_apply = precondition(first_apply)
    return (first_apply, second_apply)


def solution(mesh):
    return jax.shard_map(
        shards,
        mesh=mesh,
        in_specs=(
            P(AXES, None),
            P(AXES, None),
            P(AXES, None),
            P(AXES),
            P(AXES, None),
            P(AXES),
            P(AXES),
        ),
        out_specs=(P(AXES, None), P(AXES, None)),
        check_vma=False,
    )
```

```python
import jax
import jax.numpy as jnp
from jax import lax
from jax.sharding import PartitionSpec as P

AXES = ("sub", "grp")


def with_halo(cells, sides, width):
    for axis, dim in sides:
        count = lax.axis_size(axis)
        ends = count - 1
        head = lax.slice_in_dim(cells, 0, width, axis=dim)
        tail = lax.slice_in_dim(cells, cells.shape[dim] - width, cells.shape[dim], axis=dim)
        cells = jnp.concatenate(
            [
                lax.ppermute(tail, axis, [(i, (i + 1) % count) for i in range(ends)]),
                cells,
                lax.ppermute(head, axis, [((i + 1) % count, i) for i in range(ends)]),
            ],
            axis=dim,
        )
    return cells


def shifted(shard, axis, by):
    devices = lax.axis_size(axis)
    pairs = [(i, i + by) for i in range(devices) if 0 <= i + by < devices]
    return lax.ppermute(shard, axis, pairs)


def gather_all(block):
    count = lax.axis_size("sub") * lax.axis_size("grp")
    me = lax.axis_index("sub") * lax.axis_size("grp") + lax.axis_index("grp")
    rows = block.shape[0]
    held = lax.dynamic_update_slice_in_dim(
        jnp.zeros((count * rows, block.shape[1]), block.dtype), block, me * rows, 0
    )
    span = 1
    while span < count:
        start = (me // span) * span
        piece = lax.dynamic_slice_in_dim(held, start * rows, span * rows, 0)
        got = lax.ppermute(piece, AXES, [(i, i ^ span) for i in range(count)])
        held = lax.dynamic_update_slice_in_dim(held, got, (start ^ span) * rows, 0)
        span *= 2
    return held


def shards(resid, schur_inv, basis, scaling, coarse_inv, source_row, primal_idx):
    own_count = resid.shape[0]
    scale_column = scaling[:, None]
    primal_source = source_row[primal_idx]
    primal_scale = scaling[primal_idx][:, None]

    padded_rows = jnp.arange(3 * own_count)
    pick = (source_row[:, None] == padded_rows[None, :]).astype(jnp.bfloat16)
    spread_inv = jnp.dot(schur_inv, pick, preferred_element_type=jnp.float32).astype(jnp.bfloat16)
    spread_scale = jnp.zeros((3 * own_count,), jnp.float32).at[source_row].set(scaling)[:, None]
    places = [
        ((region * own_count + jnp.arange(own_count))[:, None] == source_row[None, :]).astype(jnp.bfloat16)
        for region in range(3)
    ]

    def select(matrix, rows):
        return jnp.dot(matrix, rows, preferred_element_type=jnp.float32)

    def precondition(vector_in):
        rounded = vector_in.astype(jnp.bfloat16)
        padded = with_halo(rounded, (("sub", 0),), own_count)
        primal = (primal_scale * padded[primal_source].astype(jnp.float32)).astype(jnp.bfloat16)
        count = lax.axis_size("sub") * lax.axis_size("grp")
        primal_all = lax.all_to_all(
            jnp.broadcast_to(primal[None], (count,) + primal.shape), AXES, 0, 0, tiled=False
        ).reshape(-1, primal.shape[1])
        scaled = (spread_scale * padded.astype(jnp.float32)).astype(jnp.bfloat16)
        solved = jnp.dot(spread_inv, scaled, preferred_element_type=jnp.float32)
        solved = lax.optimization_barrier(solved)
        coarse = jnp.dot(coarse_inv, primal_all, preferred_element_type=jnp.float32)
        coarse_rounded = coarse.astype(jnp.bfloat16)
        solved = solved + lax.dot_general(
            basis, coarse_rounded, (((0,), (0,)), ((), ())), preferred_element_type=jnp.float32
        )
        weighted = (scale_column * solved).astype(jnp.bfloat16)
        to_previous = select(places[0], weighted).astype(jnp.bfloat16)
        to_next = select(places[2], weighted).astype(jnp.bfloat16)
        from_next = shifted(to_previous, "sub", -1)
        from_previous = shifted(to_next, "sub", 1)
        kept = select(places[1], weighted).astype(jnp.bfloat16)
        return (
            kept.astype(jnp.float32)
            + from_next.astype(jnp.float32)
            + from_previous.astype(jnp.float32)
        )

    first_apply = precondition(resid)
    second_apply = precondition(first_apply)
    return (first_apply, second_apply)


def solution(mesh):
    return jax.shard_map(
        shards,
        mesh=mesh,
        in_specs=(
            P(AXES, None),
            P(AXES, None),
            P(AXES, None),
            P(AXES),
            P(AXES, None),
            P(AXES),
            P(AXES),
        ),
        out_specs=(P(AXES, None), P(AXES, None)),
        check_vma=False,
    )
```

```python
import jax
import jax.numpy as jnp
from jax import lax
from jax.experimental import pallas as pl
from jax.experimental.pallas import tpu as pltpu
from jax.sharding import PartitionSpec as P

AXES = ("sub", "grp")


def with_halo(cells, sides, width):
    for axis, dim in sides:
        count = lax.axis_size(axis)
        ends = count - 1
        head = lax.slice_in_dim(cells, 0, width, axis=dim)
        tail = lax.slice_in_dim(cells, cells.shape[dim] - width, cells.shape[dim], axis=dim)
        cells = jnp.concatenate(
            [
                lax.ppermute(tail, axis, [(i, (i + 1) % count) for i in range(ends)]),
                cells,
                lax.ppermute(head, axis, [((i + 1) % count, i) for i in range(ends)]),
            ],
            axis=dim,
        )
    return cells


def shifted(shard, axis, by):
    devices = lax.axis_size(axis)
    pairs = [(i, i + by) for i in range(devices) if 0 <= i + by < devices]
    return lax.ppermute(shard, axis, pairs)


def gather_all(block):
    count = lax.axis_size("sub") * lax.axis_size("grp")
    me = lax.axis_index("sub") * lax.axis_size("grp") + lax.axis_index("grp")
    rows = block.shape[0]
    held = lax.dynamic_update_slice_in_dim(
        jnp.zeros((count * rows, block.shape[1]), block.dtype), block, me * rows, 0
    )
    span = 1
    while span < count:
        start = (me // span) * span
        piece = lax.dynamic_slice_in_dim(held, start * rows, span * rows, 0)
        got = lax.ppermute(piece, AXES, [(i, i ^ span) for i in range(count)])
        held = lax.dynamic_update_slice_in_dim(held, got, (start ^ span) * rows, 0)
        span *= 2
    return held


def _solve_kernel(rows_ref, padded_ref, scale_ref, block_ref, out_ref, gathered_ref, scaled_ref):
    @pl.when(pl.program_id(0) == 0)
    def _():
        def body(l, carry):
            gathered_ref[pl.ds(l, 1), :] = padded_ref[pl.ds(rows_ref[l], 1), :]
            return carry

        lax.fori_loop(0, gathered_ref.shape[0], body, 0, unroll=8)
        scaled_ref[...] = (scale_ref[...] * gathered_ref[...]).astype(jnp.bfloat16)

    out_ref[...] = jnp.dot(block_ref[...], scaled_ref[...], preferred_element_type=jnp.float32)


def gather_solve(factor, padded, rows, scale_column, block=256):
    size, width = factor.shape[0], padded.shape[1]
    return pl.pallas_call(
        _solve_kernel,
        out_shape=jax.ShapeDtypeStruct((size, width), jnp.float32),
        grid_spec=pltpu.PrefetchScalarGridSpec(
            num_scalar_prefetch=1,
            grid=(size // block,),
            in_specs=[
                pl.BlockSpec(padded.shape, lambda i, r: (0, 0)),
                pl.BlockSpec(scale_column.shape, lambda i, r: (0, 0)),
                pl.BlockSpec((block, factor.shape[1]), lambda i, r: (i, 0)),
            ],
            out_specs=pl.BlockSpec((block, width), lambda i, r: (i, 0)),
            scratch_shapes=[
                pltpu.VMEM((factor.shape[1], width), jnp.float32),
                pltpu.VMEM((factor.shape[1], width), jnp.bfloat16),
            ],
        ),
        compiler_params=pltpu.CompilerParams(dimension_semantics=("arbitrary",)),
        cost_estimate=pl.CostEstimate(
            flops=2 * size * factor.shape[1] * width,
            bytes_accessed=factor.size * 2 + padded.size * 4 + size * width * 4,
            transcendentals=0,
        ),
    )(rows, padded, scale_column, factor)


def shards(resid, schur_inv, basis, scaling, coarse_inv, source_row, primal_idx):
    own_count = resid.shape[0]
    scale_column = scaling[:, None]
    primal_source = source_row[primal_idx]
    primal_scale = scaling[primal_idx][:, None]

    places = [
        ((region * own_count + jnp.arange(own_count))[:, None] == source_row[None, :]).astype(jnp.bfloat16)
        for region in range(3)
    ]

    def select(matrix, rows):
        return jnp.dot(matrix, rows, preferred_element_type=jnp.float32)

    def precondition(vector_in):
        rounded = vector_in.astype(jnp.bfloat16)
        padded = with_halo(rounded, (("sub", 0),), own_count).astype(jnp.float32)
        primal = (primal_scale * padded[primal_source]).astype(jnp.bfloat16)
        count = lax.axis_size("sub") * lax.axis_size("grp")
        primal_all = lax.all_to_all(
            jnp.broadcast_to(primal[None], (count,) + primal.shape), AXES, 0, 0, tiled=False
        ).reshape(-1, primal.shape[1])
        solved = gather_solve(schur_inv, padded, source_row, scale_column)
        coarse = jnp.dot(coarse_inv, primal_all, preferred_element_type=jnp.float32)
        coarse_rounded = coarse.astype(jnp.bfloat16)
        solved = solved + lax.dot_general(
            basis, coarse_rounded, (((0,), (0,)), ((), ())), preferred_element_type=jnp.float32
        )
        weighted = (scale_column * solved).astype(jnp.bfloat16)
        to_previous = select(places[0], weighted).astype(jnp.bfloat16)
        to_next = select(places[2], weighted).astype(jnp.bfloat16)
        from_next = shifted(to_previous, "sub", -1)
        from_previous = shifted(to_next, "sub", 1)
        kept = lax.optimization_barrier(select(places[1], weighted).astype(jnp.bfloat16))
        return (
            kept.astype(jnp.float32)
            + from_next.astype(jnp.float32)
            + from_previous.astype(jnp.float32)
        )

    first_apply = precondition(resid)
    second_apply = precondition(first_apply)
    return (first_apply, second_apply)


def solution(mesh):
    return jax.shard_map(
        shards,
        mesh=mesh,
        in_specs=(
            P(AXES, None),
            P(AXES, None),
            P(AXES, None),
            P(AXES),
            P(AXES, None),
            P(AXES),
            P(AXES),
        ),
        out_specs=(P(AXES, None), P(AXES, None)),
        check_vma=False,
    )
```

```python
import jax
import jax.numpy as jnp
from jax import lax
from jax.sharding import PartitionSpec as P

AXES = ("sub", "grp")


def with_halo(cells, sides, width):
    for axis, dim in sides:
        count = lax.axis_size(axis)
        ends = count - 1
        head = lax.slice_in_dim(cells, 0, width, axis=dim)
        tail = lax.slice_in_dim(cells, cells.shape[dim] - width, cells.shape[dim], axis=dim)
        cells = jnp.concatenate(
            [
                lax.ppermute(tail, axis, [(i, (i + 1) % count) for i in range(ends)]),
                cells,
                lax.ppermute(head, axis, [((i + 1) % count, i) for i in range(ends)]),
            ],
            axis=dim,
        )
    return cells


def shifted(shard, axis, by):
    devices = lax.axis_size(axis)
    pairs = [(i, i + by) for i in range(devices) if 0 <= i + by < devices]
    return lax.ppermute(shard, axis, pairs)


def gather_all(block):
    count = lax.axis_size("sub") * lax.axis_size("grp")
    me = lax.axis_index("sub") * lax.axis_size("grp") + lax.axis_index("grp")
    rows = block.shape[0]
    held = lax.dynamic_update_slice_in_dim(
        jnp.zeros((count * rows, block.shape[1]), block.dtype), block, me * rows, 0
    )
    span = 1
    while span < count:
        start = (me // span) * span
        piece = lax.dynamic_slice_in_dim(held, start * rows, span * rows, 0)
        got = lax.ppermute(piece, AXES, [(i, i ^ span) for i in range(count)])
        held = lax.dynamic_update_slice_in_dim(held, got, (start ^ span) * rows, 0)
        span *= 2
    return held


def shards(resid, schur_inv, basis, scaling, coarse_inv, source_row, primal_idx):
    own_count = resid.shape[0]
    scale_column = scaling[:, None]
    primal_source = source_row[primal_idx]
    primal_scale = scaling[primal_idx][:, None]

    picks = [
        (source_row[:, None] == (region * own_count + jnp.arange(own_count))[None, :]).astype(jnp.bfloat16)
        for region in range(3)
    ]
    places = [
        ((region * own_count + jnp.arange(own_count))[:, None] == source_row[None, :]).astype(jnp.bfloat16)
        for region in range(3)
    ]

    def select(matrix, rows):
        return jnp.dot(matrix, rows, preferred_element_type=jnp.float32)

    def precondition(vector_in):
        rounded = vector_in.astype(jnp.bfloat16)
        padded = with_halo(rounded, (("sub", 0),), own_count)
        before = padded[:own_count]
        after = padded[2 * own_count :]
        primal = (primal_scale * padded[primal_source].astype(jnp.float32)).astype(jnp.bfloat16)
        count = lax.axis_size("sub") * lax.axis_size("grp")
        primal_all = lax.all_to_all(
            jnp.broadcast_to(primal[None], (count,) + primal.shape), AXES, 0, 0, tiled=False
        ).reshape(-1, primal.shape[1])
        gathered = select(picks[1], rounded) + select(picks[0], before) + select(picks[2], after)
        scaled = (scale_column * gathered).astype(jnp.bfloat16)
        solved = jnp.dot(schur_inv, scaled, preferred_element_type=jnp.float32)
        solved = lax.optimization_barrier(solved)
        coarse = jnp.dot(coarse_inv, primal_all, preferred_element_type=jnp.float32)
        coarse_rounded = coarse.astype(jnp.bfloat16)
        solved = solved + lax.dot_general(
            basis, coarse_rounded, (((0,), (0,)), ((), ())), preferred_element_type=jnp.float32
        )
        weighted = (scale_column * solved).astype(jnp.bfloat16)
        to_previous = select(places[0], weighted).astype(jnp.bfloat16)
        to_next = select(places[2], weighted).astype(jnp.bfloat16)
        from_next = shifted(to_previous, "sub", -1)
        from_previous = shifted(to_next, "sub", 1)
        kept = lax.optimization_barrier(select(places[1], weighted).astype(jnp.bfloat16))
        return (
            kept.astype(jnp.float32)
            + from_next.astype(jnp.float32)
            + from_previous.astype(jnp.float32)
        )

    first_apply = precondition(resid)
    second_apply = precondition(first_apply)
    return (first_apply, second_apply)


def solution(mesh):
    return jax.shard_map(
        shards,
        mesh=mesh,
        in_specs=(
            P(AXES, None),
            P(AXES, None),
            P(AXES, None),
            P(AXES),
            P(AXES, None),
            P(AXES),
            P(AXES),
        ),
        out_specs=(P(AXES, None), P(AXES, None)),
        check_vma=False,
    )
```

```python
import jax
import jax.numpy as jnp
from jax import lax
from jax.sharding import PartitionSpec as P

AXES = ("sub", "grp")


def with_halo(cells, sides, width):
    for axis, dim in sides:
        count = lax.axis_size(axis)
        ends = count - 1
        head = lax.slice_in_dim(cells, 0, width, axis=dim)
        tail = lax.slice_in_dim(cells, cells.shape[dim] - width, cells.shape[dim], axis=dim)
        cells = jnp.concatenate(
            [
                lax.ppermute(tail, axis, [(i, (i + 1) % count) for i in range(ends)]),
                cells,
                lax.ppermute(head, axis, [((i + 1) % count, i) for i in range(ends)]),
            ],
            axis=dim,
        )
    return cells


def shifted(shard, axis, by):
    devices = lax.axis_size(axis)
    pairs = [(i, i + by) for i in range(devices) if 0 <= i + by < devices]
    return lax.ppermute(shard, axis, pairs)


def gather_all(block):
    count = lax.axis_size("sub") * lax.axis_size("grp")
    me = lax.axis_index("sub") * lax.axis_size("grp") + lax.axis_index("grp")
    rows = block.shape[0]
    held = lax.dynamic_update_slice_in_dim(
        jnp.zeros((count * rows, block.shape[1]), block.dtype), block, me * rows, 0
    )
    span = 1
    while span < count:
        start = (me // span) * span
        piece = lax.dynamic_slice_in_dim(held, start * rows, span * rows, 0)
        got = lax.ppermute(piece, AXES, [(i, i ^ span) for i in range(count)])
        held = lax.dynamic_update_slice_in_dim(held, got, (start ^ span) * rows, 0)
        span *= 2
    return held


def shards(resid, schur_inv, basis, scaling, coarse_inv, source_row, primal_idx):
    own_count = resid.shape[0]
    scale_column = scaling[:, None]
    primal_source = source_row[primal_idx]
    primal_scale = scaling[primal_idx][:, None]

    picks = [
        (source_row[:, None] == (region * own_count + jnp.arange(own_count))[None, :]).astype(jnp.bfloat16)
        for region in range(3)
    ]
    places = [
        ((region * own_count + jnp.arange(own_count))[:, None] == source_row[None, :]).astype(jnp.bfloat16)
        for region in range(3)
    ]

    def select(matrix, rows):
        return jnp.dot(matrix, rows, preferred_element_type=jnp.float32)

    def precondition(vector_in):
        rounded = vector_in.astype(jnp.bfloat16)
        padded = with_halo(rounded, (("sub", 0),), own_count)
        before = padded[:own_count]
        after = padded[2 * own_count :]
        primal = (primal_scale * padded[primal_source].astype(jnp.float32)).astype(jnp.bfloat16)
        count = lax.axis_size("sub") * lax.axis_size("grp")
        primal_all = lax.all_to_all(
            jnp.broadcast_to(primal[None], (count,) + primal.shape), AXES, 0, 0, tiled=False
        ).reshape(-1, primal.shape[1])
        gathered_own = lax.optimization_barrier(select(picks[1], rounded))
        gathered = gathered_own + select(picks[0], before) + select(picks[2], after)
        scaled = (scale_column * gathered).astype(jnp.bfloat16)
        solved = jnp.dot(schur_inv, scaled, preferred_element_type=jnp.float32)
        solved = lax.optimization_barrier(solved)
        coarse = jnp.dot(coarse_inv, primal_all, preferred_element_type=jnp.float32)
        coarse_rounded = coarse.astype(jnp.bfloat16)
        solved = solved + lax.dot_general(
            basis, coarse_rounded, (((0,), (0,)), ((), ())), preferred_element_type=jnp.float32
        )
        weighted = (scale_column * solved).astype(jnp.bfloat16)
        to_previous = select(places[0], weighted).astype(jnp.bfloat16)
        to_next = select(places[2], weighted).astype(jnp.bfloat16)
        from_next = shifted(to_previous, "sub", -1)
        from_previous = shifted(to_next, "sub", 1)
        kept = lax.optimization_barrier(select(places[1], weighted).astype(jnp.bfloat16))
        return (
            kept.astype(jnp.float32)
            + from_next.astype(jnp.float32)
            + from_previous.astype(jnp.float32)
        )

    first_apply = precondition(resid)
    second_apply = precondition(first_apply)
    return (first_apply, second_apply)


def solution(mesh):
    return jax.shard_map(
        shards,
        mesh=mesh,
        in_specs=(
            P(AXES, None),
            P(AXES, None),
            P(AXES, None),
            P(AXES),
            P(AXES, None),
            P(AXES),
            P(AXES),
        ),
        out_specs=(P(AXES, None), P(AXES, None)),
        check_vma=False,
    )
```

```python
import jax
import jax.numpy as jnp
from jax import lax
from jax.experimental import pallas as pl
from jax.experimental.pallas import tpu as pltpu
from jax.sharding import PartitionSpec as P

AXES = ("sub", "grp")


def with_halo(cells, sides, width):
    for axis, dim in sides:
        count = lax.axis_size(axis)
        ends = count - 1
        head = lax.slice_in_dim(cells, 0, width, axis=dim)
        tail = lax.slice_in_dim(cells, cells.shape[dim] - width, cells.shape[dim], axis=dim)
        cells = jnp.concatenate(
            [
                lax.ppermute(tail, axis, [(i, (i + 1) % count) for i in range(ends)]),
                cells,
                lax.ppermute(head, axis, [((i + 1) % count, i) for i in range(ends)]),
            ],
            axis=dim,
        )
    return cells


def shifted(shard, axis, by):
    devices = lax.axis_size(axis)
    pairs = [(i, i + by) for i in range(devices) if 0 <= i + by < devices]
    return lax.ppermute(shard, axis, pairs)


def gather_all(block):
    count = lax.axis_size("sub") * lax.axis_size("grp")
    me = lax.axis_index("sub") * lax.axis_size("grp") + lax.axis_index("grp")
    rows = block.shape[0]
    held = lax.dynamic_update_slice_in_dim(
        jnp.zeros((count * rows, block.shape[1]), block.dtype), block, me * rows, 0
    )
    span = 1
    while span < count:
        start = (me // span) * span
        piece = lax.dynamic_slice_in_dim(held, start * rows, span * rows, 0)
        got = lax.ppermute(piece, AXES, [(i, i ^ span) for i in range(count)])
        held = lax.dynamic_update_slice_in_dim(held, got, (start ^ span) * rows, 0)
        span *= 2
    return held


def _product_kernel(block_ref, rows_ref, out_ref):
    out_ref[...] = jnp.dot(block_ref[...], rows_ref[...], preferred_element_type=jnp.float32)


def factor_product(factor, rows, block=256):
    size, width = factor.shape[0], rows.shape[1]
    return pl.pallas_call(
        _product_kernel,
        out_shape=jax.ShapeDtypeStruct((size, width), jnp.float32),
        grid=(size // block,),
        in_specs=[
            pl.BlockSpec((block, factor.shape[1]), lambda i: (i, 0)),
            pl.BlockSpec(rows.shape, lambda i: (0, 0)),
        ],
        out_specs=pl.BlockSpec((block, width), lambda i: (i, 0)),
        cost_estimate=pl.CostEstimate(
            flops=2 * size * factor.shape[1] * width,
            bytes_accessed=factor.size * 2 + rows.size * 2 + size * width * 4,
            transcendentals=0,
        ),
    )(factor, rows)


def shards(resid, schur_inv, basis, scaling, coarse_inv, source_row, primal_idx):
    own_count = resid.shape[0]
    scale_column = scaling[:, None]
    primal_source = source_row[primal_idx]
    primal_scale = scaling[primal_idx][:, None]

    picks = [
        (source_row[:, None] == (region * own_count + jnp.arange(own_count))[None, :]).astype(jnp.bfloat16)
        for region in range(3)
    ]
    places = [
        ((region * own_count + jnp.arange(own_count))[:, None] == source_row[None, :]).astype(jnp.bfloat16)
        for region in range(3)
    ]

    def select(matrix, rows):
        return jnp.dot(matrix, rows, preferred_element_type=jnp.float32)

    def precondition(vector_in):
        rounded = vector_in.astype(jnp.bfloat16)
        padded = with_halo(rounded, (("sub", 0),), own_count)
        before = padded[:own_count]
        after = padded[2 * own_count :]
        primal = (primal_scale * padded[primal_source].astype(jnp.float32)).astype(jnp.bfloat16)
        count = lax.axis_size("sub") * lax.axis_size("grp")
        primal_all = lax.all_to_all(
            jnp.broadcast_to(primal[None], (count,) + primal.shape), AXES, 0, 0, tiled=False
        ).reshape(-1, primal.shape[1])
        gathered_own = lax.optimization_barrier(select(picks[1], rounded))
        gathered = gathered_own + select(picks[0], before) + select(picks[2], after)
        scaled = (scale_column * gathered).astype(jnp.bfloat16)
        solved = factor_product(schur_inv, scaled)
        coarse = jnp.dot(coarse_inv, primal_all, preferred_element_type=jnp.float32)
        coarse_rounded = coarse.astype(jnp.bfloat16)
        solved = solved + lax.dot_general(
            basis, coarse_rounded, (((0,), (0,)), ((), ())), preferred_element_type=jnp.float32
        )
        weighted = (scale_column * solved).astype(jnp.bfloat16)
        to_previous = select(places[0], weighted).astype(jnp.bfloat16)
        to_next = select(places[2], weighted).astype(jnp.bfloat16)
        from_next = shifted(to_previous, "sub", -1)
        from_previous = shifted(to_next, "sub", 1)
        kept = lax.optimization_barrier(select(places[1], weighted).astype(jnp.bfloat16))
        return (
            kept.astype(jnp.float32)
            + from_next.astype(jnp.float32)
            + from_previous.astype(jnp.float32)
        )

    first_apply = precondition(resid)
    second_apply = precondition(first_apply)
    return (first_apply, second_apply)


def solution(mesh):
    return jax.shard_map(
        shards,
        mesh=mesh,
        in_specs=(
            P(AXES, None),
            P(AXES, None),
            P(AXES, None),
            P(AXES),
            P(AXES, None),
            P(AXES),
            P(AXES),
        ),
        out_specs=(P(AXES, None), P(AXES, None)),
        check_vma=False,
    )
```

```python
import jax
import jax.numpy as jnp
from jax import lax
from jax.sharding import PartitionSpec as P

AXES = ("sub", "grp")


def with_halo(cells, sides, width):
    for axis, dim in sides:
        count = lax.axis_size(axis)
        ends = count - 1
        head = lax.slice_in_dim(cells, 0, width, axis=dim)
        tail = lax.slice_in_dim(cells, cells.shape[dim] - width, cells.shape[dim], axis=dim)
        cells = jnp.concatenate(
            [
                lax.ppermute(tail, axis, [(i, (i + 1) % count) for i in range(ends)]),
                cells,
                lax.ppermute(head, axis, [((i + 1) % count, i) for i in range(ends)]),
            ],
            axis=dim,
        )
    return cells


def shifted(shard, axis, by):
    devices = lax.axis_size(axis)
    pairs = [(i, i + by) for i in range(devices) if 0 <= i + by < devices]
    return lax.ppermute(shard, axis, pairs)


def gather_all(block):
    count = lax.axis_size("sub") * lax.axis_size("grp")
    me = lax.axis_index("sub") * lax.axis_size("grp") + lax.axis_index("grp")
    rows = block.shape[0]
    held = lax.dynamic_update_slice_in_dim(
        jnp.zeros((count * rows, block.shape[1]), block.dtype), block, me * rows, 0
    )
    span = 1
    while span < count:
        start = (me // span) * span
        piece = lax.dynamic_slice_in_dim(held, start * rows, span * rows, 0)
        got = lax.ppermute(piece, AXES, [(i, i ^ span) for i in range(count)])
        held = lax.dynamic_update_slice_in_dim(held, got, (start ^ span) * rows, 0)
        span *= 2
    return held


def shards(resid, schur_inv, basis, scaling, coarse_inv, source_row, primal_idx):
    own_count = resid.shape[0]
    scale_column = scaling[:, None]
    primal_source = source_row[primal_idx]
    primal_scale = scaling[primal_idx][:, None]

    picks = [
        (source_row[:, None] == (region * own_count + jnp.arange(own_count))[None, :]).astype(jnp.bfloat16)
        for region in range(3)
    ]
    places = [
        ((region * own_count + jnp.arange(own_count))[:, None] == source_row[None, :]).astype(jnp.bfloat16)
        for region in range(3)
    ]

    def select(matrix, rows):
        return jnp.dot(matrix, rows, preferred_element_type=jnp.float32)

    def precondition(vector_in):
        rounded = vector_in.astype(jnp.bfloat16)
        before = shifted(rounded, "sub", 1)
        after = shifted(rounded, "sub", -1)
        gathered_after = select(picks[2], after)
        before, gathered_after = lax.optimization_barrier((before, gathered_after))
        padded = jnp.concatenate([before, rounded, after], axis=0)
        primal = (primal_scale * padded[primal_source].astype(jnp.float32)).astype(jnp.bfloat16)
        count = lax.axis_size("sub") * lax.axis_size("grp")
        primal_all = lax.all_to_all(
            jnp.broadcast_to(primal[None], (count,) + primal.shape), AXES, 0, 0, tiled=False
        ).reshape(-1, primal.shape[1])
        gathered_own = lax.optimization_barrier(select(picks[1], rounded))
        gathered = gathered_own + select(picks[0], before) + gathered_after
        scaled = (scale_column * gathered).astype(jnp.bfloat16)
        solved = jnp.dot(schur_inv, scaled, preferred_element_type=jnp.float32)
        solved = lax.optimization_barrier(solved)
        coarse = jnp.dot(coarse_inv, primal_all, preferred_element_type=jnp.float32)
        coarse_rounded = coarse.astype(jnp.bfloat16)
        solved = solved + lax.dot_general(
            basis, coarse_rounded, (((0,), (0,)), ((), ())), preferred_element_type=jnp.float32
        )
        weighted = (scale_column * solved).astype(jnp.bfloat16)
        to_previous = select(places[0], weighted).astype(jnp.bfloat16)
        to_next = select(places[2], weighted).astype(jnp.bfloat16)
        from_next = shifted(to_previous, "sub", -1)
        from_previous = shifted(to_next, "sub", 1)
        kept = lax.optimization_barrier(select(places[1], weighted).astype(jnp.bfloat16))
        return (
            kept.astype(jnp.float32)
            + from_next.astype(jnp.float32)
            + from_previous.astype(jnp.float32)
        )

    first_apply = precondition(resid)
    second_apply = precondition(first_apply)
    return (first_apply, second_apply)


def solution(mesh):
    return jax.shard_map(
        shards,
        mesh=mesh,
        in_specs=(
            P(AXES, None),
            P(AXES, None),
            P(AXES, None),
            P(AXES),
            P(AXES, None),
            P(AXES),
            P(AXES),
        ),
        out_specs=(P(AXES, None), P(AXES, None)),
        check_vma=False,
    )
```

```python
import jax
import jax.numpy as jnp
from jax import lax
from jax.sharding import PartitionSpec as P

AXES = ("sub", "grp")


def with_halo(cells, sides, width):
    for axis, dim in sides:
        count = lax.axis_size(axis)
        ends = count - 1
        head = lax.slice_in_dim(cells, 0, width, axis=dim)
        tail = lax.slice_in_dim(cells, cells.shape[dim] - width, cells.shape[dim], axis=dim)
        cells = jnp.concatenate(
            [
                lax.ppermute(tail, axis, [(i, (i + 1) % count) for i in range(ends)]),
                cells,
                lax.ppermute(head, axis, [((i + 1) % count, i) for i in range(ends)]),
            ],
            axis=dim,
        )
    return cells


def shifted(shard, axis, by):
    devices = lax.axis_size(axis)
    pairs = [(i, i + by) for i in range(devices) if 0 <= i + by < devices]
    return lax.ppermute(shard, axis, pairs)


def gather_all(block):
    count = lax.axis_size("sub") * lax.axis_size("grp")
    me = lax.axis_index("sub") * lax.axis_size("grp") + lax.axis_index("grp")
    rows = block.shape[0]
    held = lax.dynamic_update_slice_in_dim(
        jnp.zeros((count * rows, block.shape[1]), block.dtype), block, me * rows, 0
    )
    span = 1
    while span < count:
        start = (me // span) * span
        piece = lax.dynamic_slice_in_dim(held, start * rows, span * rows, 0)
        got = lax.ppermute(piece, AXES, [(i, i ^ span) for i in range(count)])
        held = lax.dynamic_update_slice_in_dim(held, got, (start ^ span) * rows, 0)
        span *= 2
    return held


def shards(resid, schur_inv, basis, scaling, coarse_inv, source_row, primal_idx):
    own_count = resid.shape[0]
    scale_column = scaling[:, None]
    primal_source = source_row[primal_idx]
    primal_scale = scaling[primal_idx][:, None]

    picks = [
        (source_row[:, None] == (region * own_count + jnp.arange(own_count))[None, :]).astype(jnp.bfloat16)
        for region in range(3)
    ]
    places = [
        ((region * own_count + jnp.arange(own_count))[:, None] == source_row[None, :]).astype(jnp.bfloat16)
        for region in range(3)
    ]

    def select(matrix, rows):
        return jnp.dot(matrix, rows, preferred_element_type=jnp.float32)

    def precondition(vector_in):
        rounded = vector_in.astype(jnp.bfloat16)
        before = shifted(rounded, "sub", 1)
        after = shifted(rounded, "sub", -1)
        gathered_after = select(picks[2], after)
        before, gathered_after = lax.optimization_barrier((before, gathered_after))
        padded = jnp.concatenate([before, rounded, after], axis=0)
        primal = (primal_scale * padded[primal_source].astype(jnp.float32)).astype(jnp.bfloat16)
        count = lax.axis_size("sub") * lax.axis_size("grp")
        primal_copies = jnp.broadcast_to(primal[None], (count,) + primal.shape)
        primal_all = lax.all_to_all(primal_copies, AXES, 0, 0, tiled=False).reshape(-1, primal.shape[1])
        before, primal_copies = lax.optimization_barrier((before, primal_copies))
        gathered_own = lax.optimization_barrier(select(picks[1], rounded))
        gathered = gathered_own + select(picks[0], before) + gathered_after
        scaled = (scale_column * gathered).astype(jnp.bfloat16)
        solved = jnp.dot(schur_inv, scaled, preferred_element_type=jnp.float32)
        solved = lax.optimization_barrier(solved)
        coarse = jnp.dot(coarse_inv, primal_all, preferred_element_type=jnp.float32)
        coarse_rounded = coarse.astype(jnp.bfloat16)
        solved = solved + lax.dot_general(
            basis, coarse_rounded, (((0,), (0,)), ((), ())), preferred_element_type=jnp.float32
        )
        weighted = (scale_column * solved).astype(jnp.bfloat16)
        to_previous = select(places[0], weighted).astype(jnp.bfloat16)
        to_next = select(places[2], weighted).astype(jnp.bfloat16)
        from_next = shifted(to_previous, "sub", -1)
        from_previous = shifted(to_next, "sub", 1)
        kept = lax.optimization_barrier(select(places[1], weighted).astype(jnp.bfloat16))
        return (
            kept.astype(jnp.float32)
            + from_next.astype(jnp.float32)
            + from_previous.astype(jnp.float32)
        )

    first_apply = precondition(resid)
    second_apply = precondition(first_apply)
    return (first_apply, second_apply)


def solution(mesh):
    return jax.shard_map(
        shards,
        mesh=mesh,
        in_specs=(
            P(AXES, None),
            P(AXES, None),
            P(AXES, None),
            P(AXES),
            P(AXES, None),
            P(AXES),
            P(AXES),
        ),
        out_specs=(P(AXES, None), P(AXES, None)),
        check_vma=False,
    )
```

```python
import jax
import jax.numpy as jnp
from jax import lax
from jax.sharding import PartitionSpec as P

AXES = ("sub", "grp")


def with_halo(cells, sides, width):
    for axis, dim in sides:
        count = lax.axis_size(axis)
        ends = count - 1
        head = lax.slice_in_dim(cells, 0, width, axis=dim)
        tail = lax.slice_in_dim(cells, cells.shape[dim] - width, cells.shape[dim], axis=dim)
        cells = jnp.concatenate(
            [
                lax.ppermute(tail, axis, [(i, (i + 1) % count) for i in range(ends)]),
                cells,
                lax.ppermute(head, axis, [((i + 1) % count, i) for i in range(ends)]),
            ],
            axis=dim,
        )
    return cells


def shifted(shard, axis, by):
    devices = lax.axis_size(axis)
    pairs = [(i, i + by) for i in range(devices) if 0 <= i + by < devices]
    return lax.ppermute(shard, axis, pairs)


def gather_all(block):
    count = lax.axis_size("sub") * lax.axis_size("grp")
    me = lax.axis_index("sub") * lax.axis_size("grp") + lax.axis_index("grp")
    rows = block.shape[0]
    held = lax.dynamic_update_slice_in_dim(
        jnp.zeros((count * rows, block.shape[1]), block.dtype), block, me * rows, 0
    )
    span = 1
    while span < count:
        start = (me // span) * span
        piece = lax.dynamic_slice_in_dim(held, start * rows, span * rows, 0)
        got = lax.ppermute(piece, AXES, [(i, i ^ span) for i in range(count)])
        held = lax.dynamic_update_slice_in_dim(held, got, (start ^ span) * rows, 0)
        span *= 2
    return held


def shards(resid, schur_inv, basis, scaling, coarse_inv, source_row, primal_idx):
    own_count = resid.shape[0]
    scale_column = scaling[:, None]
    primal_source = source_row[primal_idx]
    primal_scale = scaling[primal_idx][:, None]

    picks = [
        (source_row[:, None] == (region * own_count + jnp.arange(own_count))[None, :]).astype(jnp.bfloat16)
        for region in range(3)
    ]
    places = [
        ((region * own_count + jnp.arange(own_count))[:, None] == source_row[None, :]).astype(jnp.bfloat16)
        for region in range(3)
    ]

    def select(matrix, rows):
        return jnp.dot(matrix, rows, preferred_element_type=jnp.float32)

    def precondition(vector_in):
        rounded = vector_in.astype(jnp.bfloat16)
        before = shifted(rounded, "sub", 1)
        after = shifted(rounded, "sub", -1)
        gathered_after = select(picks[2], after)
        before, gathered_after = lax.optimization_barrier((before, gathered_after))
        padded = jnp.concatenate([before, rounded, after], axis=0)
        primal = (primal_scale * padded[primal_source].astype(jnp.float32)).astype(jnp.bfloat16)
        group = lax.axis_size("grp")
        primal_copies = jnp.broadcast_to(primal[None], (group,) + primal.shape)
        in_group = lax.all_to_all(primal_copies, "grp", 0, 0, tiled=False)
        chain = lax.axis_size("sub")
        primal_all = lax.all_to_all(
            jnp.broadcast_to(in_group[None], (chain,) + in_group.shape), "sub", 0, 0, tiled=False
        ).reshape(-1, primal.shape[1])
        before, primal_copies = lax.optimization_barrier((before, primal_copies))
        gathered_own = lax.optimization_barrier(select(picks[1], rounded))
        gathered = gathered_own + select(picks[0], before) + gathered_after
        scaled = (scale_column * gathered).astype(jnp.bfloat16)
        solved = jnp.dot(schur_inv, scaled, preferred_element_type=jnp.float32)
        solved = lax.optimization_barrier(solved)
        coarse = jnp.dot(coarse_inv, primal_all, preferred_element_type=jnp.float32)
        coarse_rounded = coarse.astype(jnp.bfloat16)
        solved = solved + lax.dot_general(
            basis, coarse_rounded, (((0,), (0,)), ((), ())), preferred_element_type=jnp.float32
        )
        weighted = (scale_column * solved).astype(jnp.bfloat16)
        to_previous = select(places[0], weighted).astype(jnp.bfloat16)
        to_next = select(places[2], weighted).astype(jnp.bfloat16)
        from_next = shifted(to_previous, "sub", -1)
        from_previous = shifted(to_next, "sub", 1)
        kept = lax.optimization_barrier(select(places[1], weighted).astype(jnp.bfloat16))
        return (
            kept.astype(jnp.float32)
            + from_next.astype(jnp.float32)
            + from_previous.astype(jnp.float32)
        )

    first_apply = precondition(resid)
    second_apply = precondition(first_apply)
    return (first_apply, second_apply)


def solution(mesh):
    return jax.shard_map(
        shards,
        mesh=mesh,
        in_specs=(
            P(AXES, None),
            P(AXES, None),
            P(AXES, None),
            P(AXES),
            P(AXES, None),
            P(AXES),
            P(AXES),
        ),
        out_specs=(P(AXES, None), P(AXES, None)),
        check_vma=False,
    )
```

```python
import jax
import jax.numpy as jnp
from jax import lax
from jax.sharding import PartitionSpec as P

AXES = ("sub", "grp")


def with_halo(cells, sides, width):
    for axis, dim in sides:
        count = lax.axis_size(axis)
        ends = count - 1
        head = lax.slice_in_dim(cells, 0, width, axis=dim)
        tail = lax.slice_in_dim(cells, cells.shape[dim] - width, cells.shape[dim], axis=dim)
        cells = jnp.concatenate(
            [
                lax.ppermute(tail, axis, [(i, (i + 1) % count) for i in range(ends)]),
                cells,
                lax.ppermute(head, axis, [((i + 1) % count, i) for i in range(ends)]),
            ],
            axis=dim,
        )
    return cells


def shifted(shard, axis, by):
    devices = lax.axis_size(axis)
    pairs = [(i, i + by) for i in range(devices) if 0 <= i + by < devices]
    return lax.ppermute(shard, axis, pairs)


def gather_all(block):
    count = lax.axis_size("sub") * lax.axis_size("grp")
    me = lax.axis_index("sub") * lax.axis_size("grp") + lax.axis_index("grp")
    rows = block.shape[0]
    held = lax.dynamic_update_slice_in_dim(
        jnp.zeros((count * rows, block.shape[1]), block.dtype), block, me * rows, 0
    )
    span = 1
    while span < count:
        start = (me // span) * span
        piece = lax.dynamic_slice_in_dim(held, start * rows, span * rows, 0)
        got = lax.ppermute(piece, AXES, [(i, i ^ span) for i in range(count)])
        held = lax.dynamic_update_slice_in_dim(held, got, (start ^ span) * rows, 0)
        span *= 2
    return held


def shards(resid, schur_inv, basis, scaling, coarse_inv, source_row, primal_idx):
    own_count = resid.shape[0]
    scale_column = scaling[:, None]
    primal_source = source_row[primal_idx]
    primal_scale = scaling[primal_idx][:, None]

    picks = [
        (source_row[:, None] == (region * own_count + jnp.arange(own_count))[None, :]).astype(jnp.bfloat16)
        for region in range(3)
    ]
    places = [
        ((region * own_count + jnp.arange(own_count))[:, None] == source_row[None, :]).astype(jnp.bfloat16)
        for region in range(3)
    ]

    def select(matrix, rows):
        return jnp.dot(matrix, rows, preferred_element_type=jnp.float32)

    def precondition(vector_in):
        rounded = vector_in.astype(jnp.bfloat16)
        before = shifted(rounded, "sub", 1)
        after = shifted(rounded, "sub", -1)
        gathered_after = select(picks[2], after)
        before, gathered_after = lax.optimization_barrier((before, gathered_after))
        padded = jnp.concatenate([before, rounded, after], axis=0)
        primal = (primal_scale * padded[primal_source].astype(jnp.float32)).astype(jnp.bfloat16)
        count = lax.axis_size("sub") * lax.axis_size("grp")
        primal_copies = jnp.broadcast_to(primal[None], (count,) + primal.shape)
        primal_all = lax.all_to_all(primal_copies, AXES, 0, 0, tiled=False).reshape(-1, primal.shape[1])
        before, primal_copies = lax.optimization_barrier((before, primal_copies))
        gathered_own = lax.optimization_barrier(select(picks[1], rounded))
        gathered = gathered_own + select(picks[0], before) + gathered_after
        scaled = (scale_column * gathered).astype(jnp.bfloat16)
        solved = jnp.dot(schur_inv, scaled, preferred_element_type=jnp.float32)
        solved = lax.optimization_barrier(solved)
        coarse = jnp.dot(coarse_inv, primal_all, preferred_element_type=jnp.float32)
        coarse_rounded = coarse.astype(jnp.bfloat16)
        solved = solved + lax.dot_general(
            basis, coarse_rounded, (((0,), (0,)), ((), ())), preferred_element_type=jnp.float32
        )
        weighted = (scale_column * solved).astype(jnp.bfloat16)
        to_previous = select(places[0], weighted).astype(jnp.bfloat16)
        weighted_next, to_previous = lax.optimization_barrier((weighted, to_previous))
        to_next = select(places[2], weighted_next).astype(jnp.bfloat16)
        from_next = shifted(to_previous, "sub", -1)
        from_previous = shifted(to_next, "sub", 1)
        kept = lax.optimization_barrier(select(places[1], weighted).astype(jnp.bfloat16))
        return (
            kept.astype(jnp.float32)
            + from_next.astype(jnp.float32)
            + from_previous.astype(jnp.float32)
        )

    first_apply = precondition(resid)
    second_apply = precondition(first_apply)
    return (first_apply, second_apply)


def solution(mesh):
    return jax.shard_map(
        shards,
        mesh=mesh,
        in_specs=(
            P(AXES, None),
            P(AXES, None),
            P(AXES, None),
            P(AXES),
            P(AXES, None),
            P(AXES),
            P(AXES),
        ),
        out_specs=(P(AXES, None), P(AXES, None)),
        check_vma=False,
    )
```

```python
import jax
import jax.numpy as jnp
from jax import lax
from jax.sharding import PartitionSpec as P

AXES = ("sub", "grp")


def with_halo(cells, sides, width):
    for axis, dim in sides:
        count = lax.axis_size(axis)
        ends = count - 1
        head = lax.slice_in_dim(cells, 0, width, axis=dim)
        tail = lax.slice_in_dim(cells, cells.shape[dim] - width, cells.shape[dim], axis=dim)
        cells = jnp.concatenate(
            [
                lax.ppermute(tail, axis, [(i, (i + 1) % count) for i in range(ends)]),
                cells,
                lax.ppermute(head, axis, [((i + 1) % count, i) for i in range(ends)]),
            ],
            axis=dim,
        )
    return cells


def shifted(shard, axis, by):
    devices = lax.axis_size(axis)
    pairs = [(i, i + by) for i in range(devices) if 0 <= i + by < devices]
    return lax.ppermute(shard, axis, pairs)


def gather_all(block):
    count = lax.axis_size("sub") * lax.axis_size("grp")
    me = lax.axis_index("sub") * lax.axis_size("grp") + lax.axis_index("grp")
    rows = block.shape[0]
    held = lax.dynamic_update_slice_in_dim(
        jnp.zeros((count * rows, block.shape[1]), block.dtype), block, me * rows, 0
    )
    span = 1
    while span < count:
        start = (me // span) * span
        piece = lax.dynamic_slice_in_dim(held, start * rows, span * rows, 0)
        got = lax.ppermute(piece, AXES, [(i, i ^ span) for i in range(count)])
        held = lax.dynamic_update_slice_in_dim(held, got, (start ^ span) * rows, 0)
        span *= 2
    return held


def shards(resid, schur_inv, basis, scaling, coarse_inv, source_row, primal_idx):
    own_count = resid.shape[0]
    scale_column = scaling[:, None]
    primal_source = source_row[primal_idx]
    primal_scale = scaling[primal_idx][:, None]

    picks = [
        (source_row[:, None] == (region * own_count + jnp.arange(own_count))[None, :]).astype(jnp.bfloat16)
        for region in range(3)
    ]
    places = [
        ((region * own_count + jnp.arange(own_count))[:, None] == source_row[None, :]).astype(jnp.bfloat16)
        for region in range(3)
    ]

    def select(matrix, rows):
        return jnp.dot(matrix, rows, preferred_element_type=jnp.float32)

    def precondition(vector_in):
        rounded = vector_in.astype(jnp.bfloat16)
        before = shifted(rounded, "sub", 1)
        after = shifted(rounded, "sub", -1)
        gathered_after = select(picks[2], after)
        before, gathered_after = lax.optimization_barrier((before, gathered_after))
        padded = jnp.concatenate([before, rounded, after], axis=0)
        primal = (primal_scale * padded[primal_source].astype(jnp.float32)).astype(jnp.bfloat16)
        count = lax.axis_size("sub") * lax.axis_size("grp")
        primal_copies = jnp.broadcast_to(primal[None], (count,) + primal.shape)
        primal_all = lax.all_to_all(primal_copies, AXES, 0, 0, tiled=False).reshape(-1, primal.shape[1])
        before, primal_copies = lax.optimization_barrier((before, primal_copies))
        gathered_own = lax.optimization_barrier(select(picks[1], rounded))
        gathered = gathered_own + select(picks[0], before) + gathered_after
        scaled = (scale_column * gathered).astype(jnp.bfloat16)
        solved = jnp.dot(schur_inv, scaled, preferred_element_type=jnp.float32)
        solved = lax.optimization_barrier(solved)
        coarse = jnp.dot(coarse_inv, primal_all, preferred_element_type=jnp.float32)
        coarse_rounded = coarse.astype(jnp.bfloat16)
        solved = solved + lax.dot_general(
            basis, coarse_rounded, (((0,), (0,)), ((), ())), preferred_element_type=jnp.float32
        )
        weighted = (scale_column * solved).astype(jnp.bfloat16)
        to_previous = select(places[0], weighted).astype(jnp.bfloat16)
        to_next = select(places[2], weighted).astype(jnp.bfloat16)
        from_next = shifted(to_previous, "sub", -1)
        from_previous = shifted(to_next, "sub", 1)
        kept = lax.optimization_barrier(select(places[1], weighted).astype(jnp.bfloat16))
        partial = lax.optimization_barrier(kept.astype(jnp.float32) + from_next.astype(jnp.float32))
        return partial + from_previous.astype(jnp.float32)

    first_apply = precondition(resid)
    second_apply = precondition(first_apply)
    return (first_apply, second_apply)


def solution(mesh):
    return jax.shard_map(
        shards,
        mesh=mesh,
        in_specs=(
            P(AXES, None),
            P(AXES, None),
            P(AXES, None),
            P(AXES),
            P(AXES, None),
            P(AXES),
            P(AXES),
        ),
        out_specs=(P(AXES, None), P(AXES, None)),
        check_vma=False,
    )
```
